256 devices in a mesh: corpus: 32 (over z, x), group: 8 (over y, core).
Axes of the slice: x: 4, y: 4, z: 8, core: 2. Of those that a mesh axis runs over, the one named last changes fastest.
Arguments:
- embeddings: float32 [196608, 768], P(('corpus', 'group')), may hold values from -150 to 150
- labels: int32 [196608, 1], P(('corpus', 'group')), may hold values from 0 to 255, as said below
- neighbours: int32 [256], replicated, may hold values from 0 to 255, as said below
Outputs:
- dup_score: float32 [196608], P(('corpus', 'group'))
- typical: float32 [196608], P(('corpus', 'group'))
The draws below stay inside these ranges and needn't reach their ends.
Inputs may be any that keep to these rules, and one draw needn't show every extreme that they name: `labels`: in the rows of one device no cluster is named by more than 6 rows, and some cluster by exactly 6; every cluster is named by some row. `neighbours`: each cluster is the neighbour of exactly one cluster, and never its own.
All inputs are finite; a program needn't handle non-finite values.
Results may differ from the reference program's by a relative error of at most 0.0013.
Values may be sent and summed in bfloat16 or wider, within the bound.
No kernel may reach another device: no remote copies, remote signals or barrier semaphores. Data moves between devices by JAX's collectives and lax.ppermute only.
A program may use at most 128 MiB of HBM per device.

```python
import math
import jax
import jax.numpy as jnp
from jax import lax

D = 768
CLUSTERS = 256
ROWS_DEV = 768
MOST = 6
ROWS = 196608
N_CORPUS = 32
N_GROUP = 8


def cluster_chain(key):
    shuffled = jax.random.permutation(jax.random.fold_in(key, 31), CLUSTERS).astype(jnp.int32)
    following = jnp.roll(shuffled, -1)
    neighbour_of = jnp.zeros((CLUSTERS,), jnp.int32).at[shuffled].set(following)
    previous_of = jnp.zeros((CLUSTERS,), jnp.int32).at[following].set(shuffled)
    return (neighbour_of, previous_of)


def row_labels(key):
    base_key = jax.random.fold_in(key, 41)
    blocks = ROWS // ROWS_DEV
    slot_count = CLUSTERS * MOST
    slot_ids = jnp.arange(slot_count, dtype=jnp.int32)
    slot_cluster = slot_ids // MOST
    popular = jax.random.randint(jax.random.fold_in(base_key, 1), (CLUSTERS,), 0, 4, dtype=jnp.int32)
    jitter = jax.random.randint(jax.random.fold_in(base_key, 2), (blocks, slot_count), 0, 65536, dtype=jnp.int32)
    filled = jax.random.randint(jax.random.fold_in(base_key, 3), (blocks, 1), 0, CLUSTERS, dtype=jnp.int32)
    block_ids = jnp.arange(blocks, dtype=jnp.int32)[:, None]
    forced = (slot_cluster[None, :] % blocks == block_ids) & (slot_ids % MOST == 0)[None, :]
    complete = slot_cluster[None, :] == filled
    score = popular[slot_cluster][None, :] * 16384 + jitter
    score = score + jnp.where(forced, 2097152, 0) + jnp.where(complete, 4194304, 0)
    picked = jnp.argsort(-score, axis=1, stable=True)[:, :ROWS_DEV]
    chosen = slot_cluster[picked]
    mixing = jax.random.randint(jax.random.fold_in(base_key, 4), (blocks, ROWS_DEV), 0, 1073741824, dtype=jnp.int32)
    order = jnp.argsort(mixing, axis=1, stable=True)
    return jnp.take_along_axis(chosen, order, axis=1).reshape(ROWS).astype(jnp.int32)


def draw_labels(key, part):
    return row_labels(key)[:, None]


def draw_neighbours(key, part):
    return cluster_chain(key)[0]


def draw_embeddings(key, part):
    dup_slots = 4
    cluster_weight = 0.2
    labels_now = row_labels(key)
    previous_of = cluster_chain(key)[1]
    kinds = jax.random.randint(jax.random.fold_in(key, 11), (ROWS,), 0, 24, dtype=jnp.int32)
    slot_pick = jax.random.randint(jax.random.fold_in(key, 13), (ROWS,), 0, dup_slots, dtype=jnp.int32)
    source = jnp.where(kinds == 1, previous_of[labels_now], labels_now)
    copy_flag = (kinds < 2)[:, None]
    spread = jax.random.uniform(jax.random.fold_in(key, 15), (ROWS, 1), jnp.float32, 0.1, 0.33)
    key_main = jax.random.fold_in(key, 3)
    key_row = jax.random.fold_in(key, 5)
    key_col = jax.random.fold_in(key, 7)
    key_centre = jax.random.fold_in(key, 17)
    key_shared = jax.random.fold_in(key, 19)
    key_shake = jax.random.fold_in(key, 23)
    col_scale = jnp.exp(jax.random.uniform(key_col, (1, D), jnp.float32, math.log(0.5), math.log(2.0)))
    centres = jnp.clip(jax.random.normal(key_centre, (CLUSTERS, D), jnp.float32), -3.0, 3.0)
    shared = jnp.clip(jax.random.normal(key_shared, (CLUSTERS * dup_slots, D), jnp.float32), -3.0, 3.0)
    noise = jnp.clip(jax.random.normal(key_main, (ROWS, D), jnp.float32), -3.0, 3.0)
    shake = jnp.clip(jax.random.normal(key_shake, (ROWS, D), jnp.float32), -3.0, 3.0)
    row_scale = jnp.exp(jax.random.uniform(key_row, (ROWS, 1), jnp.float32, 0.0, math.log(10.0)))
    copied = shared[source * dup_slots + slot_pick] + spread * shake
    base_rows = cluster_weight * centres[source] + jnp.where(copy_flag, copied, noise)
    return base_rows * row_scale * col_scale


def setup_inputs(seed: int = 0) -> dict:
    keys = jax.random.split(jax.random.key(seed), 4)
    embeddings = draw_embeddings(jax.random.fold_in(keys[3], 71), 0)
    labels = draw_labels(jax.random.fold_in(keys[3], 71), 0)
    neighbours = draw_neighbours(jax.random.fold_in(keys[3], 71), 0)
    return dict(embeddings=embeddings, labels=labels, neighbours=neighbours)


SHARPNESS = 16.0
TYPICAL_SCALE = 8.0
EPSILON = 1e-06

def normalize(values):
    return values * lax.rsqrt(lax.optimization_barrier(jnp.sum(values * values, axis=-1, keepdims=True)) + EPSILON)

def reference(embeddings, labels, neighbours):
    unit_embed = normalize(embeddings).astype(jnp.bfloat16)
    row_label = labels[:, 0].astype(jnp.int32)
    row_total = row_label.shape[0]
    capacity = MOST * N_CORPUS * N_GROUP
    shuffled = jnp.argsort(row_label, stable=True).astype(jnp.int32)
    counts = jnp.zeros((CLUSTERS,), jnp.int32).at[row_label].add(1)
    starts = jnp.cumsum(counts) - counts
    placed = jnp.arange(row_total, dtype=jnp.int32) - starts[row_label[shuffled]]
    row_rank = jnp.zeros((row_total,), jnp.int32).at[shuffled].set(placed.astype(jnp.int32))
    padded = jnp.zeros((CLUSTERS, capacity, D), unit_embed.dtype).at[row_label, row_rank].set(unit_embed)
    slot_ids = jnp.arange(capacity, dtype=jnp.int32)
    valid = (slot_ids[None, :] < counts[:, None]).astype(jnp.float32)
    count_f = counts.astype(jnp.float32)
    distinct = slot_ids[:, None] != slot_ids[None, :]

    def per_cluster(cluster):
        other = neighbours[cluster]
        mine = padded[cluster].astype(jnp.float32)
        theirs = padded[other].astype(jnp.float32)
        g_own = jnp.dot(mine, mine.T, precision=lax.Precision.HIGHEST)
        g_near = jnp.dot(mine, theirs.T, precision=lax.Precision.HIGHEST)
        w_own = jnp.where(distinct, jnp.exp(SHARPNESS * g_own) * valid[cluster][None, :], 0.0)
        w_near = jnp.exp(SHARPNESS * g_near) * valid[other][None, :]
        own_sum = lax.optimization_barrier(jnp.sum(w_own, axis=1))
        near_sum = lax.optimization_barrier(jnp.sum(w_near, axis=1))
        return jnp.log(1.0 + own_sum / count_f[cluster] + near_sum / count_f[other])
    scores = lax.map(per_cluster, jnp.arange(CLUSTERS, dtype=jnp.int32))
    dup_score = scores[row_label, row_rank]
    unit_f = unit_embed.astype(jnp.float32)
    cluster_sums = jax.ops.segment_sum(unit_f, row_label, num_segments=CLUSTERS)
    centroid = normalize(cluster_sums)
    typical = TYPICAL_SCALE * lax.optimization_barrier(jnp.sum(unit_f * centroid[row_label], axis=1))
    return (dup_score, typical)
```

```python
import jax
import jax.numpy as jnp
from jax import lax
from jax.sharding import PartitionSpec as P

MOST = 6


SHARPNESS = 16.0
TYPICAL_SCALE = 8.0
EPSILON = 1e-06
EMPTY = 2.0


def normalize(values):
    return values * lax.rsqrt(jnp.sum(values * values, axis=-1, keepdims=True) + EPSILON)


def body(embeddings, labels, neighbours):
    axes = ("corpus", "group")
    devices = lax.axis_size("corpus") * lax.axis_size("group")
    row_count, feature_width = embeddings.shape
    clusters = neighbours.shape[0]
    per_device = clusters // devices
    slots = 2 * MOST
    unit_embed = normalize(embeddings).astype(jnp.bfloat16)
    row_label = labels[:, 0]
    cluster_ids = jnp.arange(clusters, dtype=jnp.int32)
    previous = jnp.sum(
        jnp.where(neighbours[None, :] == cluster_ids[:, None], cluster_ids[None, :], 0), axis=1
    )
    row_ids = jnp.arange(row_count, dtype=jnp.int32)
    before = (row_label[None, :] == row_label[:, None]) & (row_ids[None, :] < row_ids[:, None])
    row_slot = jnp.sum(before.astype(jnp.int32), axis=1)
    near_label = jnp.take(previous, row_label)

    member_pos = row_label * slots + row_slot
    near_pos = near_label * slots + MOST + row_slot
    slot_total = clusters * slots
    source = jnp.full((slot_total,), -1, jnp.int32)
    source = source.at[member_pos].set(row_ids).at[near_pos].set(row_ids)
    present = source >= 0
    picked = jnp.take(unit_embed, jnp.maximum(source, 0), axis=0)
    send = jnp.where(present[:, None], picked, jnp.asarray(EMPTY, jnp.bfloat16))
    send = send.reshape(devices, per_device * slots, feature_width)
    arrived = lax.all_to_all(send, axes, split_axis=0, concat_axis=0, tiled=True)
    arrived = arrived.reshape(devices, per_device, slots, feature_width)
    cluster_span = devices * MOST

    def one_cluster(rows):
        members = rows[:, :MOST].reshape(cluster_span, feature_width)
        others = rows[:, MOST:].reshape(cluster_span, feature_width)
        member_ok = members[:, 0] < 1.5
        other_ok = others[:, 0] < 1.5
        members = jnp.where(member_ok[:, None], members, jnp.zeros_like(members))
        others = jnp.where(other_ok[:, None], others, jnp.zeros_like(others))
        count_own = jnp.sum(member_ok.astype(jnp.float32))
        count_near = jnp.sum(other_ok.astype(jnp.float32))
        members_f = members.astype(jnp.float32)
        sums = jnp.sum(members_f, axis=0)
        centroid = normalize(sums)
        typical = TYPICAL_SCALE * jnp.sum(members_f * centroid[None, :], axis=1)
        g_own = lax.dot_general(
            members, members, (((1,), (1,)), ((), ())), preferred_element_type=jnp.float32
        )
        g_near = lax.dot_general(
            members, others, (((1,), (1,)), ((), ())), preferred_element_type=jnp.float32
        )
        ids = jnp.arange(cluster_span, dtype=jnp.int32)
        distinct = ids[:, None] != ids[None, :]
        w_own = jnp.where(distinct & member_ok[None, :], jnp.exp(SHARPNESS * g_own), 0.0)
        w_near = jnp.where(other_ok[None, :], jnp.exp(SHARPNESS * g_near), 0.0)
        own_sum = jnp.sum(w_own, axis=1)
        near_sum = jnp.sum(w_near, axis=1)
        score = jnp.log(1.0 + own_sum / count_own + near_sum / count_near)
        return jnp.stack(
            [score.reshape(devices, MOST), typical.reshape(devices, MOST)], axis=1
        )

    results = lax.map(one_cluster, jnp.moveaxis(arrived, 1, 0))
    payload = jnp.moveaxis(results, 1, 0).reshape(devices, per_device * 2 * MOST)
    returned = lax.all_to_all(payload, axes, split_axis=0, concat_axis=0, tiled=True)
    returned = returned.reshape(clusters, 2, MOST)
    dup_score = returned[row_label, 0, row_slot]
    typical_rows = returned[row_label, 1, row_slot]
    return (dup_score, typical_rows)


def solution(mesh):
    placed = (P(("corpus", "group"), None), P(("corpus", "group"), None), P())
    return jax.shard_map(
        body,
        mesh=mesh,
        in_specs=placed,
        out_specs=(P(("corpus", "group")), P(("corpus", "group"))),
        check_vma=False,
    )
```

```python
import jax
import jax.numpy as jnp
from jax import lax
from jax.sharding import PartitionSpec as P

MOST = 6


SHARPNESS = 16.0
TYPICAL_SCALE = 8.0
EPSILON = 1e-06
EMPTY = 2.0
PIECE = 3


def normalize(values):
    return values * lax.rsqrt(jnp.sum(values * values, axis=-1, keepdims=True) + EPSILON)


def body(embeddings, labels, neighbours):
    axes = ("corpus", "group")
    devices = lax.axis_size("corpus") * lax.axis_size("group")
    row_count, feature_width = embeddings.shape
    clusters = neighbours.shape[0]
    assert clusters == devices
    halves = MOST // PIECE
    pieces = 2 * halves
    piece_rows = clusters * PIECE
    unit_embed = normalize(embeddings).astype(jnp.bfloat16)
    row_label = labels[:, 0]
    cluster_ids = jnp.arange(clusters, dtype=jnp.int32)
    previous = jnp.sum(
        jnp.where(neighbours[None, :] == cluster_ids[:, None], cluster_ids[None, :], 0), axis=1
    )
    row_ids = jnp.arange(row_count, dtype=jnp.int32)
    before = (row_label[None, :] == row_label[:, None]) & (row_ids[None, :] < row_ids[:, None])
    row_slot = jnp.sum(before.astype(jnp.int32), axis=1)
    near_label = jnp.take(previous, row_label)

    within = row_slot % PIECE
    member_pos = (row_slot // PIECE) * piece_rows + row_label * PIECE + within
    near_pos = (halves + row_slot // PIECE) * piece_rows + near_label * PIECE + within
    slot_ids = jnp.arange(pieces * piece_rows, dtype=jnp.int32)
    chosen = (member_pos[None, :] == slot_ids[:, None]) | (near_pos[None, :] == slot_ids[:, None])
    present = jnp.any(chosen, axis=1)
    picked = lax.dot_general(
        chosen.astype(jnp.bfloat16),
        unit_embed,
        (((1,), (0,)), ((), ())),
        preferred_element_type=jnp.float32,
    )
    first = jnp.arange(feature_width, dtype=jnp.int32)[None, :] == 0
    send = jnp.where(first & ~present[:, None], EMPTY, picked).astype(jnp.bfloat16)
    send = send.reshape(pieces, piece_rows, feature_width)
    arrived = lax.all_to_all(send, axes, split_axis=1, concat_axis=1, tiled=True)
    cluster_span = halves * piece_rows
    members = arrived[:halves].reshape(cluster_span, feature_width)
    others = arrived[halves:].reshape(cluster_span, feature_width)
    member_ok = members[:, 0] < 1.5
    other_ok = others[:, 0] < 1.5
    count_own = jnp.sum(member_ok.astype(jnp.float32))
    count_near = jnp.sum(other_ok.astype(jnp.float32))
    sums = lax.dot_general(
        member_ok.astype(jnp.bfloat16)[None, :],
        members,
        (((1,), (0,)), ((), ())),
        preferred_element_type=jnp.float32,
    )
    centroid = normalize(sums)
    typical = TYPICAL_SCALE * jnp.sum(members.astype(jnp.float32) * centroid, axis=1)
    g_own = lax.dot_general(
        members, members, (((1,), (1,)), ((), ())), preferred_element_type=jnp.float32
    )
    g_near = lax.dot_general(
        members, others, (((1,), (1,)), ((), ())), preferred_element_type=jnp.float32
    )
    ids = jnp.arange(cluster_span, dtype=jnp.int32)
    distinct = ids[:, None] != ids[None, :]
    w_own = jnp.where(distinct & member_ok[None, :], jnp.exp(SHARPNESS * g_own), 0.0)
    w_near = jnp.where(other_ok[None, :], jnp.exp(SHARPNESS * g_near), 0.0)
    own_sum = jnp.sum(w_own, axis=1)
    near_sum = jnp.sum(w_near, axis=1)
    score = jnp.log(1.0 + own_sum / count_own + near_sum / count_near)
    payload = jnp.stack([score, typical]).reshape(2 * halves, piece_rows)
    returned = lax.all_to_all(payload, axes, split_axis=1, concat_axis=1, tiled=True)
    returned = returned.reshape(2, cluster_span)
    home = member_pos[:, None] == ids[None, :]
    dup_score = jnp.sum(jnp.where(home, returned[0][None, :], 0.0), axis=1)
    typical_rows = jnp.sum(jnp.where(home, returned[1][None, :], 0.0), axis=1)
    return (dup_score, typical_rows)


def solution(mesh):
    placed = (P(("corpus", "group"), None), P(("corpus", "group"), None), P())
    return jax.shard_map(
        body,
        mesh=mesh,
        in_specs=placed,
        out_specs=(P(("corpus", "group")), P(("corpus", "group"))),
        check_vma=False,
    )
```

```python
import jax
import jax.numpy as jnp
from jax import lax
from jax.sharding import PartitionSpec as P

MOST = 6


SHARPNESS = 16.0
TYPICAL_SCALE = 8.0
EPSILON = 1e-06
EMPTY = 2.0
PIECE = 3


def normalize(values):
    return values * lax.rsqrt(jnp.sum(values * values, axis=-1, keepdims=True) + EPSILON)


def body(embeddings, labels, neighbours):
    axes = ("corpus", "group")
    devices = lax.axis_size("corpus") * lax.axis_size("group")
    row_count, feature_width = embeddings.shape
    clusters = neighbours.shape[0]
    assert clusters == devices
    halves = MOST // PIECE
    pieces = 2 * halves
    piece_rows = clusters * PIECE
    unit_embed = normalize(embeddings).astype(jnp.bfloat16)
    row_label = labels[:, 0]
    cluster_ids = jnp.arange(clusters, dtype=jnp.int32)
    previous = jnp.sum(
        jnp.where(neighbours[None, :] == cluster_ids[:, None], cluster_ids[None, :], 0), axis=1
    )
    row_ids = jnp.arange(row_count, dtype=jnp.int32)
    before = (row_label[None, :] == row_label[:, None]) & (row_ids[None, :] < row_ids[:, None])
    row_slot = jnp.sum(before.astype(jnp.int32), axis=1)
    label_hot = row_label[:, None] == cluster_ids[None, :]
    near_label = jnp.sum(jnp.where(label_hot, previous[None, :], 0), axis=1)
    local_count = jnp.sum(label_hot.astype(jnp.int32), axis=0)
    near_count = jnp.sum(
        jnp.where(neighbours[:, None] == cluster_ids[None, :], local_count[None, :], 0), axis=1
    )

    within = row_slot % PIECE
    half = row_slot // PIECE
    member_pos = (row_label * PIECE + within) * pieces + half
    near_pos = (near_label * PIECE + within) * pieces + halves + half
    slot_ids = jnp.arange(pieces * piece_rows, dtype=jnp.int32)
    chosen = (member_pos[None, :] == slot_ids[:, None]) | (near_pos[None, :] == slot_ids[:, None])
    slot_piece = slot_ids % pieces
    slot_rank = (slot_piece % halves) * PIECE + (slot_ids // pieces) % PIECE
    slot_cluster = slot_ids // (pieces * PIECE)
    have = jnp.where(slot_piece < halves, local_count[slot_cluster], near_count[slot_cluster])
    present = have > slot_rank
    picked = lax.dot_general(
        chosen.astype(jnp.bfloat16),
        unit_embed,
        (((1,), (0,)), ((), ())),
        preferred_element_type=jnp.float32,
    )
    first = jnp.arange(feature_width, dtype=jnp.int32)[None, :] == 0
    send = jnp.where(first & ~present[:, None], EMPTY, picked).astype(jnp.bfloat16)
    send = send.reshape(piece_rows, pieces, feature_width).transpose(1, 0, 2)
    arrived = lax.all_to_all(send, axes, split_axis=1, concat_axis=1, tiled=True)
    cluster_span = halves * piece_rows
    members = arrived[:halves].reshape(cluster_span, feature_width)
    others = arrived[halves:].reshape(cluster_span, feature_width)
    member_ok = members[:, 0] < 1.5
    other_ok = others[:, 0] < 1.5
    count_own = jnp.sum(member_ok.astype(jnp.float32))
    count_near = jnp.sum(other_ok.astype(jnp.float32))
    sums = lax.dot_general(
        member_ok.astype(jnp.bfloat16)[None, :],
        members,
        (((1,), (0,)), ((), ())),
        preferred_element_type=jnp.float32,
    )
    centroid = normalize(sums)
    typical = TYPICAL_SCALE * jnp.sum(members.astype(jnp.float32) * centroid, axis=1)
    g_own = lax.dot_general(
        members, members, (((1,), (1,)), ((), ())), preferred_element_type=jnp.float32
    )
    g_near = lax.dot_general(
        members, others, (((1,), (1,)), ((), ())), preferred_element_type=jnp.float32
    )
    ids = jnp.arange(cluster_span, dtype=jnp.int32)
    distinct = ids[:, None] != ids[None, :]
    w_own = jnp.where(distinct & member_ok[None, :], jnp.exp(SHARPNESS * g_own), 0.0)
    w_near = jnp.where(other_ok[None, :], jnp.exp(SHARPNESS * g_near), 0.0)
    own_sum = jnp.sum(w_own, axis=1)
    near_sum = jnp.sum(w_near, axis=1)
    score = jnp.log(1.0 + own_sum / count_own + near_sum / count_near)

    def by_source(values):
        return values.reshape(halves, clusters, PIECE).transpose(1, 0, 2).reshape(clusters, MOST)

    payload = jnp.stack([by_source(score), by_source(typical)], axis=1).reshape(clusters, 2 * MOST)
    returned = lax.all_to_all(payload, axes, split_axis=0, concat_axis=0, tiled=True)
    returned = returned.reshape(clusters, 2, MOST)
    home = (row_label * MOST + row_slot)[:, None] == ids[None, :]
    dup_score = jnp.sum(jnp.where(home, returned[:, 0].reshape(-1)[None, :], 0.0), axis=1)
    typical_rows = jnp.sum(jnp.where(home, returned[:, 1].reshape(-1)[None, :], 0.0), axis=1)
    return (dup_score, typical_rows)


def solution(mesh):
    placed = (P(("corpus", "group"), None), P(("corpus", "group"), None), P())
    return jax.shard_map(
        body,
        mesh=mesh,
        in_specs=placed,
        out_specs=(P(("corpus", "group")), P(("corpus", "group"))),
        check_vma=False,
    )
```

```python
import jax
import jax.numpy as jnp
from jax import lax
from jax.sharding import PartitionSpec as P

MOST = 6


SHARPNESS = 16.0
TYPICAL_SCALE = 8.0
EPSILON = 1e-06
EMPTY = 2.0
PIECE = 3


def normalize(values):
    return values * lax.rsqrt(jnp.sum(values * values, axis=-1, keepdims=True) + EPSILON)


def body(embeddings, labels, neighbours):
    axes = ("corpus", "group")
    devices = lax.axis_size("corpus") * lax.axis_size("group")
    row_count, feature_width = embeddings.shape
    clusters = neighbours.shape[0]
    assert clusters == devices
    halves = MOST // PIECE
    pieces = 2 * halves
    piece_rows = clusters * PIECE
    unit_embed = normalize(embeddings).astype(jnp.bfloat16)
    row_label = labels[:, 0]
    cluster_ids = jnp.arange(clusters, dtype=jnp.int32)
    previous = jnp.sum(
        jnp.where(neighbours[None, :] == cluster_ids[:, None], cluster_ids[None, :], 0), axis=1
    )
    row_ids = jnp.arange(row_count, dtype=jnp.int32)
    before = (row_label[None, :] == row_label[:, None]) & (row_ids[None, :] < row_ids[:, None])
    row_slot = jnp.sum(before.astype(jnp.int32), axis=1)
    label_hot = row_label[:, None] == cluster_ids[None, :]
    near_label = jnp.sum(jnp.where(label_hot, previous[None, :], 0), axis=1)
    local_count = jnp.sum(label_hot.astype(jnp.int32), axis=0)
    near_count = jnp.sum(
        jnp.where(neighbours[:, None] == cluster_ids[None, :], local_count[None, :], 0), axis=1
    )

    within = row_slot % PIECE
    half = row_slot // PIECE
    member_pos = half * piece_rows + row_label * PIECE + within
    near_pos = (halves + half) * piece_rows + near_label * PIECE + within
    slot_ids = jnp.arange(pieces * piece_rows, dtype=jnp.int32)
    chosen = (member_pos[None, :] == slot_ids[:, None]) | (near_pos[None, :] == slot_ids[:, None])
    shape3 = (pieces, clusters, PIECE)
    piece_at = lax.broadcasted_iota(jnp.int32, shape3, 0)
    k_at = lax.broadcasted_iota(jnp.int32, shape3, 2)
    have = jnp.where(
        piece_at < halves,
        jnp.broadcast_to(local_count[None, :, None], shape3),
        jnp.broadcast_to(near_count[None, :, None], shape3),
    )
    present = (have > (piece_at % halves) * PIECE + k_at).reshape(-1)
    picked = lax.dot_general(
        chosen.astype(jnp.bfloat16),
        unit_embed,
        (((1,), (0,)), ((), ())),
        preferred_element_type=jnp.float32,
    )
    first = jnp.arange(feature_width, dtype=jnp.int32)[None, :] == 0
    send = jnp.where(first & ~present[:, None], EMPTY, picked).astype(jnp.bfloat16)
    send = send.reshape(pieces, piece_rows, feature_width)
    arrived = lax.all_to_all(send, axes, split_axis=1, concat_axis=1, tiled=True)
    cluster_span = halves * piece_rows
    members = arrived[:halves].reshape(cluster_span, feature_width)
    others = arrived[halves:].reshape(cluster_span, feature_width)
    member_ok = members[:, 0] < 1.5
    other_ok = others[:, 0] < 1.5
    count_own = jnp.sum(member_ok.astype(jnp.float32))
    count_near = jnp.sum(other_ok.astype(jnp.float32))
    sums = lax.dot_general(
        member_ok.astype(jnp.bfloat16)[None, :],
        members,
        (((1,), (0,)), ((), ())),
        preferred_element_type=jnp.float32,
    )
    centroid = normalize(sums)
    typical = TYPICAL_SCALE * jnp.sum(members.astype(jnp.float32) * centroid, axis=1)
    g_own = lax.dot_general(
        members, members, (((1,), (1,)), ((), ())), preferred_element_type=jnp.float32
    )
    g_near = lax.dot_general(
        members, others, (((1,), (1,)), ((), ())), preferred_element_type=jnp.float32
    )
    ids = jnp.arange(cluster_span, dtype=jnp.int32)
    distinct = ids[:, None] != ids[None, :]
    w_own = jnp.where(distinct & member_ok[None, :], jnp.exp(SHARPNESS * g_own), 0.0)
    w_near = jnp.where(other_ok[None, :], jnp.exp(SHARPNESS * g_near), 0.0)
    own_sum = jnp.sum(w_own, axis=1)
    near_sum = jnp.sum(w_near, axis=1)
    score = jnp.log(1.0 + own_sum / count_own + near_sum / count_near)

    def by_source(values):
        return values.reshape(halves, clusters, PIECE).transpose(1, 0, 2).reshape(clusters, MOST)

    payload = jnp.stack([by_source(score), by_source(typical)], axis=1).reshape(clusters, 2 * MOST)
    returned = lax.all_to_all(payload, axes, split_axis=0, concat_axis=0, tiled=True)
    returned = returned.reshape(clusters, 2, MOST)
    home = (row_label * MOST + row_slot)[:, None] == ids[None, :]
    dup_score = jnp.sum(jnp.where(home, returned[:, 0].reshape(-1)[None, :], 0.0), axis=1)
    typical_rows = jnp.sum(jnp.where(home, returned[:, 1].reshape(-1)[None, :], 0.0), axis=1)
    return (dup_score, typical_rows)


def solution(mesh):
    placed = (P(("corpus", "group"), None), P(("corpus", "group"), None), P())
    return jax.shard_map(
        body,
        mesh=mesh,
        in_specs=placed,
        out_specs=(P(("corpus", "group")), P(("corpus", "group"))),
        check_vma=False,
    )
```

```python
import jax
import jax.numpy as jnp
from jax import lax
from jax.sharding import PartitionSpec as P

MOST = 6


SHARPNESS = 16.0
TYPICAL_SCALE = 8.0
EPSILON = 1e-06
EMPTY = 2.0
PIECE = 3


def normalize(values):
    return values * lax.rsqrt(jnp.sum(values * values, axis=-1, keepdims=True) + EPSILON)


def body(embeddings, labels, neighbours):
    axes = ("corpus", "group")
    devices = lax.axis_size("corpus") * lax.axis_size("group")
    row_count, feature_width = embeddings.shape
    clusters = neighbours.shape[0]
    assert clusters == devices
    halves = MOST // PIECE
    pieces = 2 * halves
    piece_rows = clusters * PIECE
    unit_embed = normalize(embeddings).astype(jnp.bfloat16)
    row_label = labels[:, 0]
    cluster_ids = jnp.arange(clusters, dtype=jnp.int32)
    previous = jnp.sum(
        jnp.where(neighbours[None, :] == cluster_ids[:, None], cluster_ids[None, :], 0), axis=1
    )
    row_ids = jnp.arange(row_count, dtype=jnp.int32)
    before = (row_label[None, :] == row_label[:, None]) & (row_ids[None, :] < row_ids[:, None])
    row_slot = jnp.sum(before.astype(jnp.int32), axis=1)
    label_hot = row_label[:, None] == cluster_ids[None, :]
    near_label = jnp.sum(jnp.where(label_hot, previous[None, :], 0), axis=1)
    local_count = jnp.sum(label_hot.astype(jnp.int32), axis=0)
    near_count = jnp.sum(
        jnp.where(neighbours[:, None] == cluster_ids[None, :], local_count[None, :], 0), axis=1
    )

    within = row_slot % PIECE
    half = row_slot // PIECE
    member_pos = half * piece_rows + row_label * PIECE + within
    near_pos = (halves + half) * piece_rows + near_label * PIECE + within
    slot_ids = jnp.arange(pieces * piece_rows, dtype=jnp.int32)
    chosen = (member_pos[None, :] == slot_ids[:, None]) | (near_pos[None, :] == slot_ids[:, None])
    shape3 = (pieces, clusters, PIECE)
    piece_at = lax.broadcasted_iota(jnp.int32, shape3, 0)
    k_at = lax.broadcasted_iota(jnp.int32, shape3, 2)
    have = jnp.where(
        piece_at < halves,
        jnp.broadcast_to(local_count[None, :, None], shape3),
        jnp.broadcast_to(near_count[None, :, None], shape3),
    )
    present = (have > (piece_at % halves) * PIECE + k_at).reshape(-1)
    picked = lax.dot_general(
        chosen.astype(jnp.bfloat16),
        unit_embed,
        (((1,), (0,)), ((), ())),
        preferred_element_type=jnp.float32,
    )
    first = jnp.arange(feature_width, dtype=jnp.int32)[None, :] == 0
    send = jnp.where(first & ~present[:, None], EMPTY, picked).astype(jnp.bfloat16)
    send = send.reshape(pieces, piece_rows, feature_width)
    arrived = lax.all_to_all(send, axes, split_axis=1, concat_axis=1, tiled=True)
    cluster_span = halves * piece_rows
    members = arrived[:halves]
    others = arrived[halves:]
    member_ok = members[:, :, 0] < 1.5
    other_ok = others[:, :, 0] < 1.5
    count_own = jnp.sum(member_ok.astype(jnp.float32))
    count_near = jnp.sum(other_ok.astype(jnp.float32))
    sums = lax.dot_general(
        member_ok.astype(jnp.bfloat16),
        members,
        (((0, 1), (0, 1)), ((), ())),
        preferred_element_type=jnp.float32,
    )
    centroid = normalize(sums)
    typical = TYPICAL_SCALE * jnp.sum(members.astype(jnp.float32) * centroid, axis=2).reshape(-1)
    g_own = lax.dot_general(
        members, members, (((2,), (2,)), ((), ())), preferred_element_type=jnp.float32
    ).reshape(cluster_span, cluster_span)
    g_near = lax.dot_general(
        members, others, (((2,), (2,)), ((), ())), preferred_element_type=jnp.float32
    ).reshape(cluster_span, cluster_span)
    ids = jnp.arange(cluster_span, dtype=jnp.int32)
    distinct = ids[:, None] != ids[None, :]
    member_ok = member_ok.reshape(-1)
    other_ok = other_ok.reshape(-1)
    w_own = jnp.where(distinct & member_ok[None, :], jnp.exp(SHARPNESS * g_own), 0.0)
    w_near = jnp.where(other_ok[None, :], jnp.exp(SHARPNESS * g_near), 0.0)
    own_sum = jnp.sum(w_own, axis=1)
    near_sum = jnp.sum(w_near, axis=1)
    score = jnp.log(1.0 + own_sum / count_own + near_sum / count_near)

    def by_source(values):
        return values.reshape(halves, clusters, PIECE).transpose(1, 0, 2).reshape(clusters, MOST)

    payload = jnp.stack([by_source(score), by_source(typical)], axis=1).reshape(clusters, 2 * MOST)
    returned = lax.all_to_all(payload, axes, split_axis=0, concat_axis=0, tiled=True)
    returned = returned.reshape(clusters, 2, MOST)
    home = (row_label * MOST + row_slot)[:, None] == ids[None, :]
    dup_score = jnp.sum(jnp.where(home, returned[:, 0].reshape(-1)[None, :], 0.0), axis=1)
    typical_rows = jnp.sum(jnp.where(home, returned[:, 1].reshape(-1)[None, :], 0.0), axis=1)
    return (dup_score, typical_rows)


def solution(mesh):
    placed = (P(("corpus", "group"), None), P(("corpus", "group"), None), P())
    return jax.shard_map(
        body,
        mesh=mesh,
        in_specs=placed,
        out_specs=(P(("corpus", "group")), P(("corpus", "group"))),
        check_vma=False,
    )
```

```python
import functools

import jax
import jax.numpy as jnp
from jax import lax
from jax.experimental import pallas as pl
from jax.sharding import PartitionSpec as P

MOST = 6


SHARPNESS = 16.0
TYPICAL_SCALE = 8.0
EPSILON = 1e-06
EMPTY = 2.0
PIECE = 3


def normalize(values):
    return values * lax.rsqrt(jnp.sum(values * values, axis=-1, keepdims=True) + EPSILON)


def pair_kernel(rows_ref, ok_ref, centroid_ref, score_ref, typical_ref, *, halves, block):
    piece_rows = rows_ref.shape[1]
    step = pl.program_id(0)
    per_piece = piece_rows // block
    first_row = (step % per_piece) * block
    queries = rows_ref[step // per_piece, pl.ds(first_row, block), :]
    row_at = (step // per_piece) * piece_rows + first_row + lax.broadcasted_iota(
        jnp.int32, (block, piece_rows), 0
    )
    col_at = lax.broadcasted_iota(jnp.int32, (block, piece_rows), 1)
    own = jnp.zeros((block, 1), jnp.float32)
    near = jnp.zeros((block, 1), jnp.float32)
    for piece in range(halves):
        cols = slice(piece * piece_rows, (piece + 1) * piece_rows)
        g_own = lax.dot_general(
            queries, rows_ref[piece], (((1,), (1,)), ((), ())), preferred_element_type=jnp.float32
        )
        keep = (ok_ref[0:1, cols] > 0.5) & (col_at + piece * piece_rows != row_at)
        own = own + jnp.sum(jnp.where(keep, jnp.exp(SHARPNESS * g_own), 0.0), axis=1, keepdims=True)
        g_near = lax.dot_general(
            queries,
            rows_ref[halves + piece],
            (((1,), (1,)), ((), ())),
            preferred_element_type=jnp.float32,
        )
        keep = ok_ref[1:2, cols] > 0.5
        near = near + jnp.sum(jnp.where(keep, jnp.exp(SHARPNESS * g_near), 0.0), axis=1, keepdims=True)
    count_own = jnp.sum(ok_ref[0:1, :], axis=1, keepdims=True)
    count_near = jnp.sum(ok_ref[1:2, :], axis=1, keepdims=True)
    score_ref[...] = jnp.log(1.0 + own / count_own + near / count_near)
    typical_ref[...] = TYPICAL_SCALE * jnp.sum(
        queries.astype(jnp.float32) * centroid_ref[...], axis=1, keepdims=True
    )


def pair_scores(arrived, member_ok, other_ok, centroid, halves, block=256):
    pieces, piece_rows, feature_width = arrived.shape
    span = halves * piece_rows
    oks = jnp.stack([member_ok, other_ok]).astype(jnp.float32)
    out = jax.ShapeDtypeStruct((span, 1), jnp.float32)
    score, typical = pl.pallas_call(
        functools.partial(pair_kernel, halves=halves, block=block),
        grid=(span // block,),
        in_specs=[
            pl.BlockSpec((pieces, piece_rows, feature_width), lambda i: (0, 0, 0)),
            pl.BlockSpec((2, span), lambda i: (0, 0)),
            pl.BlockSpec((1, feature_width), lambda i: (0, 0)),
        ],
        out_specs=[pl.BlockSpec((block, 1), lambda i: (i, 0))] * 2,
        out_shape=[out, out],
    )(arrived, oks, centroid.reshape(1, feature_width))
    return score[:, 0], typical[:, 0]


def body(embeddings, labels, neighbours):
    axes = ("corpus", "group")
    devices = lax.axis_size("corpus") * lax.axis_size("group")
    row_count, feature_width = embeddings.shape
    clusters = neighbours.shape[0]
    assert clusters == devices
    halves = MOST // PIECE
    pieces = 2 * halves
    piece_rows = clusters * PIECE
    unit_embed = normalize(embeddings).astype(jnp.bfloat16)
    row_label = labels[:, 0]
    cluster_ids = jnp.arange(clusters, dtype=jnp.int32)
    previous = jnp.sum(
        jnp.where(neighbours[None, :] == cluster_ids[:, None], cluster_ids[None, :], 0), axis=1
    )
    row_ids = jnp.arange(row_count, dtype=jnp.int32)
    before = (row_label[None, :] == row_label[:, None]) & (row_ids[None, :] < row_ids[:, None])
    row_slot = jnp.sum(before.astype(jnp.int32), axis=1)
    label_hot = row_label[:, None] == cluster_ids[None, :]
    near_label = jnp.sum(jnp.where(label_hot, previous[None, :], 0), axis=1)
    local_count = jnp.sum(label_hot.astype(jnp.int32), axis=0)
    near_count = jnp.sum(
        jnp.where(neighbours[:, None] == cluster_ids[None, :], local_count[None, :], 0), axis=1
    )

    within = row_slot % PIECE
    half = row_slot // PIECE
    member_pos = half * piece_rows + row_label * PIECE + within
    near_pos = (halves + half) * piece_rows + near_label * PIECE + within
    slot_ids = jnp.arange(pieces * piece_rows, dtype=jnp.int32)
    chosen = (member_pos[None, :] == slot_ids[:, None]) | (near_pos[None, :] == slot_ids[:, None])
    shape3 = (pieces, clusters, PIECE)
    piece_at = lax.broadcasted_iota(jnp.int32, shape3, 0)
    k_at = lax.broadcasted_iota(jnp.int32, shape3, 2)
    have = jnp.where(
        piece_at < halves,
        jnp.broadcast_to(local_count[None, :, None], shape3),
        jnp.broadcast_to(near_count[None, :, None], shape3),
    )
    present = (have > (piece_at % halves) * PIECE + k_at).reshape(-1)
    picked = lax.dot_general(
        chosen.astype(jnp.bfloat16),
        unit_embed,
        (((1,), (0,)), ((), ())),
        preferred_element_type=jnp.float32,
    )
    first = jnp.arange(feature_width, dtype=jnp.int32)[None, :] == 0
    send = jnp.where(first & ~present[:, None], EMPTY, picked).astype(jnp.bfloat16)
    send = send.reshape(pieces, piece_rows, feature_width)
    arrived = lax.all_to_all(send, axes, split_axis=1, concat_axis=1, tiled=True)
    cluster_span = halves * piece_rows
    member_ok = (arrived[:halves, :, 0] < 1.5).reshape(-1)
    other_ok = (arrived[halves:, :, 0] < 1.5).reshape(-1)
    members = arrived[:halves].reshape(cluster_span, feature_width)
    sums = lax.dot_general(
        member_ok.astype(jnp.bfloat16)[None, :],
        members,
        (((1,), (0,)), ((), ())),
        preferred_element_type=jnp.float32,
    )
    centroid = normalize(sums)
    score, typical = pair_scores(arrived, member_ok, other_ok, centroid, halves)
    ids = jnp.arange(cluster_span, dtype=jnp.int32)

    def by_source(values):
        return values.reshape(halves, clusters, PIECE).transpose(1, 0, 2).reshape(clusters, MOST)

    payload = jnp.stack([by_source(score), by_source(typical)], axis=1).reshape(clusters, 2 * MOST)
    returned = lax.all_to_all(payload, axes, split_axis=0, concat_axis=0, tiled=True)
    returned = returned.reshape(clusters, 2, MOST)
    home = (row_label * MOST + row_slot)[:, None] == ids[None, :]
    dup_score = jnp.sum(jnp.where(home, returned[:, 0].reshape(-1)[None, :], 0.0), axis=1)
    typical_rows = jnp.sum(jnp.where(home, returned[:, 1].reshape(-1)[None, :], 0.0), axis=1)
    return (dup_score, typical_rows)


def solution(mesh):
    placed = (P(("corpus", "group"), None), P(("corpus", "group"), None), P())
    return jax.shard_map(
        body,
        mesh=mesh,
        in_specs=placed,
        out_specs=(P(("corpus", "group")), P(("corpus", "group"))),
        check_vma=False,
    )
```

```python
import jax
import jax.numpy as jnp
from jax import lax
from jax.sharding import PartitionSpec as P

MOST = 6


SHARPNESS = 16.0
TYPICAL_SCALE = 8.0
EPSILON = 1e-06
EMPTY = 2.0
PIECE = 3


def normalize(values):
    return values * lax.rsqrt(jnp.sum(values * values, axis=-1, keepdims=True) + EPSILON)


def body(embeddings, labels, neighbours):
    axes = ("corpus", "group")
    devices = lax.axis_size("corpus") * lax.axis_size("group")
    row_count, feature_width = embeddings.shape
    clusters = neighbours.shape[0]
    assert clusters == devices
    halves = MOST // PIECE
    pieces = 2 * halves
    piece_rows = clusters * PIECE
    unit_embed = normalize(embeddings).astype(jnp.bfloat16)
    row_label = labels[:, 0]
    cluster_ids = jnp.arange(clusters, dtype=jnp.int32)
    row_ids = jnp.arange(row_count, dtype=jnp.int32)
    before = (row_label[None, :] == row_label[:, None]) & (row_ids[None, :] < row_ids[:, None])
    row_slot = jnp.sum(before.astype(jnp.int32), axis=1)
    label_hot = row_label[:, None] == cluster_ids[None, :]
    local_count = jnp.sum(label_hot.astype(jnp.int32), axis=0)

    within = row_slot % PIECE
    half = row_slot // PIECE
    member_pos = half * piece_rows + row_label * PIECE + within
    slot_ids = jnp.arange(halves * piece_rows, dtype=jnp.int32)
    chosen = member_pos[None, :] == slot_ids[:, None]
    shape3 = (halves, clusters, PIECE)
    half_at = lax.broadcasted_iota(jnp.int32, shape3, 0)
    k_at = lax.broadcasted_iota(jnp.int32, shape3, 2)
    have = jnp.broadcast_to(local_count[None, :, None], shape3)
    present = (have > half_at * PIECE + k_at).reshape(-1)
    picked = lax.dot_general(
        chosen.astype(jnp.bfloat16),
        unit_embed,
        (((1,), (0,)), ((), ())),
        preferred_element_type=jnp.float32,
    )
    first = jnp.arange(feature_width, dtype=jnp.int32)[None, :] == 0
    member_send = jnp.where(first & ~present[:, None], EMPTY, picked).astype(jnp.bfloat16)
    member_send = member_send.reshape(halves, clusters, PIECE * feature_width)
    follow = (neighbours[:, None] == cluster_ids[None, :]).astype(jnp.bfloat16)
    near_send = lax.dot_general(
        follow, member_send, (((1,), (1,)), ((), ())), preferred_element_type=jnp.float32
    ).astype(jnp.bfloat16)
    near_send = near_send.transpose(1, 0, 2)
    send = jnp.concatenate([member_send, near_send], axis=0)
    send = send.reshape(pieces, piece_rows, feature_width)
    arrived = lax.all_to_all(send, axes, split_axis=1, concat_axis=1, tiled=True)
    cluster_span = halves * piece_rows
    members = arrived[:halves].reshape(cluster_span, feature_width)
    others = arrived[halves:].reshape(cluster_span, feature_width)
    member_ok = members[:, 0] < 1.5
    other_ok = others[:, 0] < 1.5
    count_own = jnp.sum(member_ok.astype(jnp.float32))
    count_near = jnp.sum(other_ok.astype(jnp.float32))
    sums = lax.dot_general(
        member_ok.astype(jnp.bfloat16)[None, :],
        members,
        (((1,), (0,)), ((), ())),
        preferred_element_type=jnp.float32,
    )
    centroid = normalize(sums)
    typical = TYPICAL_SCALE * jnp.sum(members.astype(jnp.float32) * centroid, axis=1)
    g_own = lax.dot_general(
        members, members, (((1,), (1,)), ((), ())), preferred_element_type=jnp.float32
    )
    g_near = lax.dot_general(
        members, others, (((1,), (1,)), ((), ())), preferred_element_type=jnp.float32
    )
    ids = jnp.arange(cluster_span, dtype=jnp.int32)
    distinct = ids[:, None] != ids[None, :]
    w_own = jnp.where(distinct & member_ok[None, :], jnp.exp(SHARPNESS * g_own), 0.0)
    w_near = jnp.where(other_ok[None, :], jnp.exp(SHARPNESS * g_near), 0.0)
    own_sum = jnp.sum(w_own, axis=1)
    near_sum = jnp.sum(w_near, axis=1)
    score = jnp.log(1.0 + own_sum / count_own + near_sum / count_near)

    def by_source(values):
        return values.reshape(halves, clusters, PIECE).transpose(1, 0, 2).reshape(clusters, MOST)

    payload = jnp.stack([by_source(score), by_source(typical)], axis=1).reshape(clusters, 2 * MOST)
    returned = lax.all_to_all(payload, axes, split_axis=0, concat_axis=0, tiled=True)
    returned = returned.reshape(clusters, 2, MOST)
    home = (row_label * MOST + row_slot)[:, None] == ids[None, :]
    dup_score = jnp.sum(jnp.where(home, returned[:, 0].reshape(-1)[None, :], 0.0), axis=1)
    typical_rows = jnp.sum(jnp.where(home, returned[:, 1].reshape(-1)[None, :], 0.0), axis=1)
    return (dup_score, typical_rows)


def solution(mesh):
    placed = (P(("corpus", "group"), None), P(("corpus", "group"), None), P())
    return jax.shard_map(
        body,
        mesh=mesh,
        in_specs=placed,
        out_specs=(P(("corpus", "group")), P(("corpus", "group"))),
        check_vma=False,
    )
```

```python
import jax
import jax.numpy as jnp
from jax import lax
from jax.sharding import PartitionSpec as P

MOST = 6


SHARPNESS = 16.0
TYPICAL_SCALE = 8.0
EPSILON = 1e-06
EMPTY = 2.0
PIECE = 3


def normalize(values):
    return values * lax.rsqrt(jnp.sum(values * values, axis=-1, keepdims=True) + EPSILON)


def body(embeddings, labels, neighbours):
    axes = ("corpus", "group")
    devices = lax.axis_size("corpus") * lax.axis_size("group")
    row_count, feature_width = embeddings.shape
    clusters = neighbours.shape[0]
    assert clusters == devices
    halves = MOST // PIECE
    pieces = 2 * halves
    piece_rows = clusters * PIECE
    unit_embed = normalize(embeddings).astype(jnp.bfloat16)
    row_label = labels[:, 0]
    cluster_ids = jnp.arange(clusters, dtype=jnp.int32)
    previous = jnp.sum(
        jnp.where(neighbours[None, :] == cluster_ids[:, None], cluster_ids[None, :], 0), axis=1
    )
    row_ids = jnp.arange(row_count, dtype=jnp.int32)
    before = (row_label[None, :] == row_label[:, None]) & (row_ids[None, :] < row_ids[:, None])
    row_slot = jnp.sum(before.astype(jnp.int32), axis=1)
    label_hot = row_label[:, None] == cluster_ids[None, :]
    near_label = jnp.sum(jnp.where(label_hot, previous[None, :], 0), axis=1)
    local_count = jnp.sum(label_hot.astype(jnp.int32), axis=0)
    near_count = jnp.sum(
        jnp.where(neighbours[:, None] == cluster_ids[None, :], local_count[None, :], 0), axis=1
    )

    within = row_slot % PIECE
    half = row_slot // PIECE
    member_pos = half * piece_rows + row_label * PIECE + within
    near_pos = (halves + half) * piece_rows + near_label * PIECE + within
    slot_ids = jnp.arange(pieces * piece_rows, dtype=jnp.int32)
    chosen = (member_pos[None, :] == slot_ids[:, None]) | (near_pos[None, :] == slot_ids[:, None])
    shape3 = (pieces, clusters, PIECE)
    piece_at = lax.broadcasted_iota(jnp.int32, shape3, 0)
    k_at = lax.broadcasted_iota(jnp.int32, shape3, 2)
    have = jnp.where(
        piece_at < halves,
        jnp.broadcast_to(local_count[None, :, None], shape3),
        jnp.broadcast_to(near_count[None, :, None], shape3),
    )
    present = (have > (piece_at % halves) * PIECE + k_at).reshape(-1)
    picked = lax.dot_general(
        chosen.astype(jnp.bfloat16),
        unit_embed,
        (((1,), (0,)), ((), ())),
        preferred_element_type=jnp.float32,
    )
    first = jnp.arange(feature_width, dtype=jnp.int32)[None, :] == 0
    send = jnp.where(first & ~present[:, None], EMPTY, picked).astype(jnp.bfloat16)
    send = send.reshape(pieces, piece_rows, feature_width)
    arrived = lax.all_to_all(send, axes, split_axis=1, concat_axis=1, tiled=True)
    cluster_span = halves * piece_rows
    parts = [arrived[p] for p in range(pieces)]
    oks = [part[:, 0] < 1.5 for part in parts]
    member_ok = jnp.concatenate(oks[:halves])
    other_ok = jnp.concatenate(oks[halves:])
    count_own = jnp.sum(member_ok.astype(jnp.float32))
    count_near = jnp.sum(other_ok.astype(jnp.float32))
    sums = sum(
        lax.dot_general(
            oks[h].astype(jnp.bfloat16)[None, :],
            parts[h],
            (((1,), (0,)), ((), ())),
            preferred_element_type=jnp.float32,
        )
        for h in range(halves)
    )
    centroid = normalize(sums)
    typical = jnp.concatenate(
        [TYPICAL_SCALE * jnp.sum(parts[h].astype(jnp.float32) * centroid, axis=1) for h in range(halves)]
    )
    ids = jnp.arange(cluster_span, dtype=jnp.int32)
    local = jnp.arange(piece_rows, dtype=jnp.int32)
    same = local[:, None] == local[None, :]

    def weights(queries, keys, ok, mask_self):
        g = lax.dot_general(
            queries, keys, (((1,), (1,)), ((), ())), preferred_element_type=jnp.float32
        )
        keep = ok[None, :] & ~same if mask_self else jnp.broadcast_to(ok[None, :], g.shape)
        return jnp.sum(jnp.where(keep, jnp.exp(SHARPNESS * g), 0.0), axis=1)

    own_sum = jnp.concatenate(
        [
            sum(weights(parts[h], parts[j], oks[j], h == j) for j in range(halves))
            for h in range(halves)
        ]
    )
    near_sum = jnp.concatenate(
        [
            sum(weights(parts[h], parts[halves + j], oks[halves + j], False) for j in range(halves))
            for h in range(halves)
        ]
    )
    score = jnp.log(1.0 + own_sum / count_own + near_sum / count_near)

    def by_source(values):
        return values.reshape(halves, clusters, PIECE).transpose(1, 0, 2).reshape(clusters, MOST)

    payload = jnp.stack([by_source(score), by_source(typical)], axis=1).reshape(clusters, 2 * MOST)
    returned = lax.all_to_all(payload, axes, split_axis=0, concat_axis=0, tiled=True)
    returned = returned.reshape(clusters, 2, MOST)
    home = (row_label * MOST + row_slot)[:, None] == ids[None, :]
    dup_score = jnp.sum(jnp.where(home, returned[:, 0].reshape(-1)[None, :], 0.0), axis=1)
    typical_rows = jnp.sum(jnp.where(home, returned[:, 1].reshape(-1)[None, :], 0.0), axis=1)
    return (dup_score, typical_rows)


def solution(mesh):
    placed = (P(("corpus", "group"), None), P(("corpus", "group"), None), P())
    return jax.shard_map(
        body,
        mesh=mesh,
        in_specs=placed,
        out_specs=(P(("corpus", "group")), P(("corpus", "group"))),
        check_vma=False,
    )
```

```python
import jax
import jax.numpy as jnp
from jax import lax
from jax.experimental.layout import Layout, with_layout_constraint
from jax.sharding import PartitionSpec as P

MOST = 6


SHARPNESS = 16.0
TYPICAL_SCALE = 8.0
EPSILON = 1e-06
EMPTY = 2.0
PIECE = 3


def normalize(values):
    return values * lax.rsqrt(jnp.sum(values * values, axis=-1, keepdims=True) + EPSILON)


def body(embeddings, labels, neighbours):
    axes = ("corpus", "group")
    devices = lax.axis_size("corpus") * lax.axis_size("group")
    row_count, feature_width = embeddings.shape
    clusters = neighbours.shape[0]
    assert clusters == devices
    halves = MOST // PIECE
    pieces = 2 * halves
    piece_rows = clusters * PIECE
    unit_embed = normalize(embeddings).astype(jnp.bfloat16)
    row_label = labels[:, 0]
    cluster_ids = jnp.arange(clusters, dtype=jnp.int32)
    previous = jnp.sum(
        jnp.where(neighbours[None, :] == cluster_ids[:, None], cluster_ids[None, :], 0), axis=1
    )
    row_ids = jnp.arange(row_count, dtype=jnp.int32)
    before = (row_label[None, :] == row_label[:, None]) & (row_ids[None, :] < row_ids[:, None])
    row_slot = jnp.sum(before.astype(jnp.int32), axis=1)
    label_hot = row_label[:, None] == cluster_ids[None, :]
    near_label = jnp.sum(jnp.where(label_hot, previous[None, :], 0), axis=1)
    local_count = jnp.sum(label_hot.astype(jnp.int32), axis=0)
    near_count = jnp.sum(
        jnp.where(neighbours[:, None] == cluster_ids[None, :], local_count[None, :], 0), axis=1
    )

    within = row_slot % PIECE
    half = row_slot // PIECE
    member_pos = half * piece_rows + row_label * PIECE + within
    near_pos = (halves + half) * piece_rows + near_label * PIECE + within
    slot_ids = jnp.arange(pieces * piece_rows, dtype=jnp.int32).reshape(pieces, piece_rows)
    chosen = (member_pos[None, None, :] == slot_ids[:, :, None]) | (
        near_pos[None, None, :] == slot_ids[:, :, None]
    )
    shape3 = (pieces, clusters, PIECE)
    piece_at = lax.broadcasted_iota(jnp.int32, shape3, 0)
    k_at = lax.broadcasted_iota(jnp.int32, shape3, 2)
    have = jnp.where(
        piece_at < halves,
        jnp.broadcast_to(local_count[None, :, None], shape3),
        jnp.broadcast_to(near_count[None, :, None], shape3),
    )
    present = (have > (piece_at % halves) * PIECE + k_at).reshape(pieces, piece_rows)
    picked = lax.dot_general(
        chosen.astype(jnp.bfloat16),
        unit_embed,
        (((2,), (0,)), ((), ())),
        preferred_element_type=jnp.float32,
    )
    first = jnp.arange(feature_width, dtype=jnp.int32)[None, None, :] == 0
    send = jnp.where(first & ~present[:, :, None], EMPTY, picked).astype(jnp.bfloat16)
    send = with_layout_constraint(send, Layout(major_to_minor=(1, 0, 2)))
    arrived = lax.all_to_all(send, axes, split_axis=1, concat_axis=1, tiled=True)
    cluster_span = halves * piece_rows
    members = arrived[:halves].reshape(cluster_span, feature_width)
    others = arrived[halves:].reshape(cluster_span, feature_width)
    member_ok = members[:, 0] < 1.5
    other_ok = others[:, 0] < 1.5
    count_own = jnp.sum(member_ok.astype(jnp.float32))
    count_near = jnp.sum(other_ok.astype(jnp.float32))
    sums = lax.dot_general(
        member_ok.astype(jnp.bfloat16)[None, :],
        members,
        (((1,), (0,)), ((), ())),
        preferred_element_type=jnp.float32,
    )
    centroid = normalize(sums)
    typical = TYPICAL_SCALE * jnp.sum(members.astype(jnp.float32) * centroid, axis=1)
    g_own = lax.dot_general(
        members, members, (((1,), (1,)), ((), ())), preferred_element_type=jnp.float32
    )
    g_near = lax.dot_general(
        members, others, (((1,), (1,)), ((), ())), preferred_element_type=jnp.float32
    )
    ids = jnp.arange(cluster_span, dtype=jnp.int32)
    distinct = ids[:, None] != ids[None, :]
    w_own = jnp.where(distinct & member_ok[None, :], jnp.exp(SHARPNESS * g_own), 0.0)
    w_near = jnp.where(other_ok[None, :], jnp.exp(SHARPNESS * g_near), 0.0)
    own_sum = jnp.sum(w_own, axis=1)
    near_sum = jnp.sum(w_near, axis=1)
    score = jnp.log(1.0 + own_sum / count_own + near_sum / count_near)

    def by_source(values):
        return values.reshape(halves, clusters, PIECE).transpose(1, 0, 2).reshape(clusters, MOST)

    payload = jnp.stack([by_source(score), by_source(typical)], axis=1).reshape(clusters, 2 * MOST)
    returned = lax.all_to_all(payload, axes, split_axis=0, concat_axis=0, tiled=True)
    returned = returned.reshape(clusters, 2, MOST)
    home = (row_label * MOST + row_slot)[:, None] == ids[None, :]
    dup_score = jnp.sum(jnp.where(home, returned[:, 0].reshape(-1)[None, :], 0.0), axis=1)
    typical_rows = jnp.sum(jnp.where(home, returned[:, 1].reshape(-1)[None, :], 0.0), axis=1)
    return (dup_score, typical_rows)


def solution(mesh):
    placed = (P(("corpus", "group"), None), P(("corpus", "group"), None), P())
    return jax.shard_map(
        body,
        mesh=mesh,
        in_specs=placed,
        out_specs=(P(("corpus", "group")), P(("corpus", "group"))),
        check_vma=False,
    )
```

```python
import jax
import jax.numpy as jnp
from jax import lax
from jax.sharding import PartitionSpec as P

MOST = 6


SHARPNESS = 16.0
TYPICAL_SCALE = 8.0
EPSILON = 1e-06
EMPTY = 2.0
PIECE = 6


def normalize(values):
    return values * lax.rsqrt(jnp.sum(values * values, axis=-1, keepdims=True) + EPSILON)


def body(embeddings, labels, neighbours):
    axes = ("corpus", "group")
    devices = lax.axis_size("corpus") * lax.axis_size("group")
    row_count, feature_width = embeddings.shape
    clusters = neighbours.shape[0]
    assert clusters == devices
    halves = MOST // PIECE
    pieces = 2 * halves
    piece_rows = clusters * PIECE
    unit_embed = normalize(embeddings).astype(jnp.bfloat16)
    row_label = labels[:, 0]
    cluster_ids = jnp.arange(clusters, dtype=jnp.int32)
    previous = jnp.sum(
        jnp.where(neighbours[None, :] == cluster_ids[:, None], cluster_ids[None, :], 0), axis=1
    )
    row_ids = jnp.arange(row_count, dtype=jnp.int32)
    before = (row_label[None, :] == row_label[:, None]) & (row_ids[None, :] < row_ids[:, None])
    row_slot = jnp.sum(before.astype(jnp.int32), axis=1)
    label_hot = row_label[:, None] == cluster_ids[None, :]
    near_label = jnp.sum(jnp.where(label_hot, previous[None, :], 0), axis=1)
    local_count = jnp.sum(label_hot.astype(jnp.int32), axis=0)
    near_count = jnp.sum(
        jnp.where(neighbours[:, None] == cluster_ids[None, :], local_count[None, :], 0), axis=1
    )

    within = row_slot % PIECE
    half = row_slot // PIECE
    member_pos = half * piece_rows + row_label * PIECE + within
    near_pos = (halves + half) * piece_rows + near_label * PIECE + within
    slot_ids = jnp.arange(pieces * piece_rows, dtype=jnp.int32)
    chosen = (member_pos[None, :] == slot_ids[:, None]) | (near_pos[None, :] == slot_ids[:, None])
    shape3 = (pieces, clusters, PIECE)
    piece_at = lax.broadcasted_iota(jnp.int32, shape3, 0)
    k_at = lax.broadcasted_iota(jnp.int32, shape3, 2)
    have = jnp.where(
        piece_at < halves,
        jnp.broadcast_to(local_count[None, :, None], shape3),
        jnp.broadcast_to(near_count[None, :, None], shape3),
    )
    present = (have > (piece_at % halves) * PIECE + k_at).reshape(-1)
    picked = lax.dot_general(
        chosen.astype(jnp.bfloat16),
        unit_embed,
        (((1,), (0,)), ((), ())),
        preferred_element_type=jnp.float32,
    )
    first = jnp.arange(feature_width, dtype=jnp.int32)[None, :] == 0
    send = jnp.where(first & ~present[:, None], EMPTY, picked).astype(jnp.bfloat16)
    send = send.reshape(pieces, piece_rows, feature_width)
    arrived = lax.all_to_all(send, axes, split_axis=1, concat_axis=1, tiled=True)
    cluster_span = halves * piece_rows
    members = arrived[:halves].reshape(cluster_span, feature_width)
    others = arrived[halves:].reshape(cluster_span, feature_width)
    member_ok = members[:, 0] < 1.5
    other_ok = others[:, 0] < 1.5
    count_own = jnp.sum(member_ok.astype(jnp.float32))
    count_near = jnp.sum(other_ok.astype(jnp.float32))
    sums = lax.dot_general(
        member_ok.astype(jnp.bfloat16)[None, :],
        members,
        (((1,), (0,)), ((), ())),
        preferred_element_type=jnp.float32,
    )
    centroid = normalize(sums)
    typical = TYPICAL_SCALE * jnp.sum(members.astype(jnp.float32) * centroid, axis=1)
    g_own = lax.dot_general(
        members, members, (((1,), (1,)), ((), ())), preferred_element_type=jnp.float32
    )
    g_near = lax.dot_general(
        members, others, (((1,), (1,)), ((), ())), preferred_element_type=jnp.float32
    )
    ids = jnp.arange(cluster_span, dtype=jnp.int32)
    distinct = ids[:, None] != ids[None, :]
    w_own = jnp.where(distinct & member_ok[None, :], jnp.exp(SHARPNESS * g_own), 0.0)
    w_near = jnp.where(other_ok[None, :], jnp.exp(SHARPNESS * g_near), 0.0)
    own_sum = jnp.sum(w_own, axis=1)
    near_sum = jnp.sum(w_near, axis=1)
    score = jnp.log(1.0 + own_sum / count_own + near_sum / count_near)

    def by_source(values):
        return values.reshape(halves, clusters, PIECE).transpose(1, 0, 2).reshape(clusters, MOST)

    payload = jnp.stack([by_source(score), by_source(typical)], axis=1).reshape(clusters, 2 * MOST)
    returned = lax.all_to_all(payload, axes, split_axis=0, concat_axis=0, tiled=True)
    returned = returned.reshape(clusters, 2, MOST)
    home = (row_label * MOST + row_slot)[:, None] == ids[None, :]
    dup_score = jnp.sum(jnp.where(home, returned[:, 0].reshape(-1)[None, :], 0.0), axis=1)
    typical_rows = jnp.sum(jnp.where(home, returned[:, 1].reshape(-1)[None, :], 0.0), axis=1)
    return (dup_score, typical_rows)


def solution(mesh):
    placed = (P(("corpus", "group"), None), P(("corpus", "group"), None), P())
    return jax.shard_map(
        body,
        mesh=mesh,
        in_specs=placed,
        out_specs=(P(("corpus", "group")), P(("corpus", "group"))),
        check_vma=False,
    )
```

```python
import jax
import jax.numpy as jnp
from jax import lax
from jax.sharding import PartitionSpec as P

MOST = 6


SHARPNESS = 16.0
TYPICAL_SCALE = 8.0
EPSILON = 1e-06
EMPTY = 2.0
PIECE = 3


def normalize(values):
    return values * lax.rsqrt(jnp.sum(values * values, axis=-1, keepdims=True) + EPSILON)


def body(embeddings, labels, neighbours):
    axes = ("corpus", "group")
    devices = lax.axis_size("corpus") * lax.axis_size("group")
    row_count, feature_width = embeddings.shape
    clusters = neighbours.shape[0]
    assert clusters == devices
    halves = MOST // PIECE
    pieces = 2 * halves
    piece_rows = clusters * PIECE
    unit_embed = normalize(embeddings).astype(jnp.bfloat16)
    row_label = labels[:, 0]
    cluster_ids = jnp.arange(clusters, dtype=jnp.int32)
    previous = jnp.sum(
        jnp.where(neighbours[None, :] == cluster_ids[:, None], cluster_ids[None, :], 0), axis=1
    )
    row_ids = jnp.arange(row_count, dtype=jnp.int32)
    before = (row_label[None, :] == row_label[:, None]) & (row_ids[None, :] < row_ids[:, None])
    row_slot = jnp.sum(before.astype(jnp.int32), axis=1)
    label_hot = row_label[:, None] == cluster_ids[None, :]
    near_label = jnp.sum(jnp.where(label_hot, previous[None, :], 0), axis=1)
    local_count = jnp.sum(label_hot.astype(jnp.int32), axis=0)
    near_count = jnp.sum(
        jnp.where(neighbours[:, None] == cluster_ids[None, :], local_count[None, :], 0), axis=1
    )

    within = row_slot % PIECE
    half = row_slot // PIECE
    member_pos = half * piece_rows + row_label * PIECE + within
    near_pos = (halves + half) * piece_rows + near_label * PIECE + within
    slot_ids = jnp.arange(pieces * piece_rows, dtype=jnp.int32)
    chosen = (member_pos[None, :] == slot_ids[:, None]) | (near_pos[None, :] == slot_ids[:, None])
    shape3 = (pieces, clusters, PIECE)
    piece_at = lax.broadcasted_iota(jnp.int32, shape3, 0)
    k_at = lax.broadcasted_iota(jnp.int32, shape3, 2)
    have = jnp.where(
        piece_at < halves,
        jnp.broadcast_to(local_count[None, :, None], shape3),
        jnp.broadcast_to(near_count[None, :, None], shape3),
    )
    present = (have > (piece_at % halves) * PIECE + k_at).reshape(-1)
    picked = lax.dot_general(
        chosen.astype(jnp.bfloat16),
        unit_embed,
        (((1,), (0,)), ((), ())),
        preferred_element_type=jnp.float32,
    )
    first = jnp.arange(feature_width, dtype=jnp.int32)[None, :] == 0
    send = jnp.where(first & ~present[:, None], EMPTY, picked).astype(jnp.bfloat16)
    send = send.reshape(pieces, piece_rows, feature_width)
    arrived = lax.all_to_all(send, axes, split_axis=1, concat_axis=1, tiled=True)
    cluster_span = halves * piece_rows
    keys = arrived.reshape(pieces * piece_rows, feature_width)
    members = keys[:cluster_span]
    key_ok = keys[:, 0] < 1.5
    member_ok = key_ok[:cluster_span]
    count_own = jnp.sum(member_ok.astype(jnp.float32))
    count_near = jnp.sum(key_ok[cluster_span:].astype(jnp.float32))
    sums = lax.dot_general(
        member_ok.astype(jnp.bfloat16)[None, :],
        members,
        (((1,), (0,)), ((), ())),
        preferred_element_type=jnp.float32,
    )
    centroid = normalize(sums)
    typical = TYPICAL_SCALE * jnp.sum(members.astype(jnp.float32) * centroid, axis=1)
    g = lax.dot_general(
        members, keys, (((1,), (1,)), ((), ())), preferred_element_type=jnp.float32
    )
    ids = jnp.arange(cluster_span, dtype=jnp.int32)
    col_ids = jnp.arange(pieces * piece_rows, dtype=jnp.int32)
    weights = jnp.exp(SHARPNESS * g)
    own_keep = (col_ids[None, :] < cluster_span) & (col_ids[None, :] != ids[:, None]) & key_ok[None, :]
    near_keep = (col_ids[None, :] >= cluster_span) & key_ok[None, :]
    own_sum = jnp.sum(jnp.where(own_keep, weights, 0.0), axis=1)
    near_sum = jnp.sum(jnp.where(near_keep, weights, 0.0), axis=1)
    score = jnp.log(1.0 + own_sum / count_own + near_sum / count_near)

    def by_source(values):
        return values.reshape(halves, clusters, PIECE).transpose(1, 0, 2).reshape(clusters, MOST)

    payload = jnp.stack([by_source(score), by_source(typical)], axis=1).reshape(clusters, 2 * MOST)
    returned = lax.all_to_all(payload, axes, split_axis=0, concat_axis=0, tiled=True)
    returned = returned.reshape(clusters, 2, MOST)
    home = (row_label * MOST + row_slot)[:, None] == ids[None, :]
    dup_score = jnp.sum(jnp.where(home, returned[:, 0].reshape(-1)[None, :], 0.0), axis=1)
    typical_rows = jnp.sum(jnp.where(home, returned[:, 1].reshape(-1)[None, :], 0.0), axis=1)
    return (dup_score, typical_rows)


def solution(mesh):
    placed = (P(("corpus", "group"), None), P(("corpus", "group"), None), P())
    return jax.shard_map(
        body,
        mesh=mesh,
        in_specs=placed,
        out_specs=(P(("corpus", "group")), P(("corpus", "group"))),
        check_vma=False,
    )
```

```python
import jax
import jax.numpy as jnp
from jax import lax
from jax.sharding import PartitionSpec as P

MOST = 6


SHARPNESS = 16.0
TYPICAL_SCALE = 8.0
EPSILON = 1e-06
EMPTY = 2.0
PIECE = 3


def normalize(values):
    return values * lax.rsqrt(jnp.sum(values * values, axis=-1, keepdims=True) + EPSILON)


def body(embeddings, labels, neighbours):
    axes = ("corpus", "group")
    devices = lax.axis_size("corpus") * lax.axis_size("group")
    row_count, feature_width = embeddings.shape
    clusters = neighbours.shape[0]
    assert clusters == devices
    halves = MOST // PIECE
    pieces = 2 * halves
    piece_rows = clusters * PIECE
    unit_embed = normalize(embeddings).astype(jnp.bfloat16)
    row_label = labels[:, 0]
    cluster_ids = jnp.arange(clusters, dtype=jnp.int32)
    previous = jnp.sum(
        jnp.where(neighbours[None, :] == cluster_ids[:, None], cluster_ids[None, :], 0), axis=1
    )
    row_ids = jnp.arange(row_count, dtype=jnp.int32)
    before = (row_label[None, :] == row_label[:, None]) & (row_ids[None, :] < row_ids[:, None])
    row_slot = jnp.sum(before.astype(jnp.int32), axis=1)
    label_hot = row_label[:, None] == cluster_ids[None, :]
    near_label = jnp.sum(jnp.where(label_hot, previous[None, :], 0), axis=1)
    local_count = jnp.sum(label_hot.astype(jnp.int32), axis=0)
    near_count = jnp.sum(
        jnp.where(neighbours[:, None] == cluster_ids[None, :], local_count[None, :], 0), axis=1
    )

    within = row_slot % PIECE
    half = row_slot // PIECE
    member_pos = half * piece_rows + row_label * PIECE + within
    near_pos = (halves + half) * piece_rows + near_label * PIECE + within
    slot_ids = jnp.arange(pieces * piece_rows, dtype=jnp.int32)
    chosen = (member_pos[None, :] == slot_ids[:, None]) | (near_pos[None, :] == slot_ids[:, None])
    shape3 = (pieces, clusters, PIECE)
    piece_at = lax.broadcasted_iota(jnp.int32, shape3, 0)
    k_at = lax.broadcasted_iota(jnp.int32, shape3, 2)
    have = jnp.where(
        piece_at < halves,
        jnp.broadcast_to(local_count[None, :, None], shape3),
        jnp.broadcast_to(near_count[None, :, None], shape3),
    )
    present = (have > (piece_at % halves) * PIECE + k_at).reshape(-1)
    picked = lax.dot_general(
        chosen.astype(jnp.bfloat16),
        unit_embed,
        (((1,), (0,)), ((), ())),
        preferred_element_type=jnp.float32,
    )
    first = jnp.arange(feature_width, dtype=jnp.int32)[None, :] == 0
    send = jnp.where(first & ~present[:, None], EMPTY, picked).astype(jnp.bfloat16)
    split_width = feature_width // 2
    send = send.reshape(pieces, piece_rows, 2, split_width).transpose(0, 2, 1, 3)
    send = send.reshape(2 * pieces, piece_rows, split_width)
    arrived = lax.all_to_all(send, axes, split_axis=1, concat_axis=1, tiled=True)
    arrived = arrived.reshape(pieces, 2, piece_rows, split_width).transpose(0, 2, 1, 3)
    arrived = arrived.reshape(pieces, piece_rows, feature_width)
    cluster_span = halves * piece_rows
    members = arrived[:halves].reshape(cluster_span, feature_width)
    others = arrived[halves:].reshape(cluster_span, feature_width)
    member_ok = members[:, 0] < 1.5
    other_ok = others[:, 0] < 1.5
    count_own = jnp.sum(member_ok.astype(jnp.float32))
    count_near = jnp.sum(other_ok.astype(jnp.float32))
    sums = lax.dot_general(
        member_ok.astype(jnp.bfloat16)[None, :],
        members,
        (((1,), (0,)), ((), ())),
        preferred_element_type=jnp.float32,
    )
    centroid = normalize(sums)
    typical = TYPICAL_SCALE * jnp.sum(members.astype(jnp.float32) * centroid, axis=1)
    g_own = lax.dot_general(
        members, members, (((1,), (1,)), ((), ())), preferred_element_type=jnp.float32
    )
    g_near = lax.dot_general(
        members, others, (((1,), (1,)), ((), ())), preferred_element_type=jnp.float32
    )
    ids = jnp.arange(cluster_span, dtype=jnp.int32)
    distinct = ids[:, None] != ids[None, :]
    w_own = jnp.where(distinct & member_ok[None, :], jnp.exp(SHARPNESS * g_own), 0.0)
    w_near = jnp.where(other_ok[None, :], jnp.exp(SHARPNESS * g_near), 0.0)
    own_sum = jnp.sum(w_own, axis=1)
    near_sum = jnp.sum(w_near, axis=1)
    score = jnp.log(1.0 + own_sum / count_own + near_sum / count_near)

    def by_source(values):
        return values.reshape(halves, clusters, PIECE).transpose(1, 0, 2).reshape(clusters, MOST)

    payload = jnp.stack([by_source(score), by_source(typical)], axis=1).reshape(clusters, 2 * MOST)
    returned = lax.all_to_all(payload, axes, split_axis=0, concat_axis=0, tiled=True)
    returned = returned.reshape(clusters, 2, MOST)
    home = (row_label * MOST + row_slot)[:, None] == ids[None, :]
    dup_score = jnp.sum(jnp.where(home, returned[:, 0].reshape(-1)[None, :], 0.0), axis=1)
    typical_rows = jnp.sum(jnp.where(home, returned[:, 1].reshape(-1)[None, :], 0.0), axis=1)
    return (dup_score, typical_rows)


def solution(mesh):
    placed = (P(("corpus", "group"), None), P(("corpus", "group"), None), P())
    return jax.shard_map(
        body,
        mesh=mesh,
        in_specs=placed,
        out_specs=(P(("corpus", "group")), P(("corpus", "group"))),
        check_vma=False,
    )
```

```python
import jax
import jax.numpy as jnp
from jax import lax
from jax.sharding import PartitionSpec as P

MOST = 6


SHARPNESS = 16.0
TYPICAL_SCALE = 8.0
EPSILON = 1e-06
EMPTY = 2.0
PIECE = 3


def normalize(values):
    return values * lax.rsqrt(jnp.sum(values * values, axis=-1, keepdims=True) + EPSILON)


def body(embeddings, labels, neighbours):
    axes = ("corpus", "group")
    devices = lax.axis_size("corpus") * lax.axis_size("group")
    row_count, feature_width = embeddings.shape
    clusters = neighbours.shape[0]
    assert clusters == devices
    halves = MOST // PIECE
    pieces = 2 * halves
    piece_rows = clusters * PIECE
    unit_embed = normalize(embeddings).astype(jnp.bfloat16)
    row_label = labels[:, 0]
    cluster_ids = jnp.arange(clusters, dtype=jnp.int32)
    previous = jnp.sum(
        jnp.where(neighbours[None, :] == cluster_ids[:, None], cluster_ids[None, :], 0), axis=1
    )
    row_ids = jnp.arange(row_count, dtype=jnp.int32)
    before = (row_label[None, :] == row_label[:, None]) & (row_ids[None, :] < row_ids[:, None])
    row_slot = jnp.sum(before.astype(jnp.int32), axis=1)
    label_hot = row_label[:, None] == cluster_ids[None, :]
    near_label = jnp.sum(jnp.where(label_hot, previous[None, :], 0), axis=1)
    local_count = jnp.sum(label_hot.astype(jnp.int32), axis=0)
    near_count = jnp.sum(
        jnp.where(neighbours[:, None] == cluster_ids[None, :], local_count[None, :], 0), axis=1
    )

    within = row_slot % PIECE
    half = row_slot // PIECE
    member_pos = half * piece_rows + row_label * PIECE + within
    near_pos = (halves + half) * piece_rows + near_label * PIECE + within
    slot_ids = jnp.arange(pieces * piece_rows, dtype=jnp.int32)
    chosen = (member_pos[None, :] == slot_ids[:, None]) | (near_pos[None, :] == slot_ids[:, None])
    shape3 = (pieces, clusters, PIECE)
    piece_at = lax.broadcasted_iota(jnp.int32, shape3, 0)
    k_at = lax.broadcasted_iota(jnp.int32, shape3, 2)
    have = jnp.where(
        piece_at < halves,
        jnp.broadcast_to(local_count[None, :, None], shape3),
        jnp.broadcast_to(near_count[None, :, None], shape3),
    )
    present = (have > (piece_at % halves) * PIECE + k_at).reshape(-1)
    picked = lax.dot_general(
        chosen.astype(jnp.bfloat16),
        unit_embed,
        (((1,), (0,)), ((), ())),
        preferred_element_type=jnp.float32,
    )
    first = jnp.arange(feature_width, dtype=jnp.int32)[None, :] == 0
    send = jnp.where(first & ~present[:, None], EMPTY, picked).astype(jnp.bfloat16)
    send = send.reshape(pieces, piece_rows, feature_width).transpose(1, 0, 2)
    arrived = lax.all_to_all(send, axes, split_axis=0, concat_axis=0, tiled=True)
    arrived = arrived.transpose(1, 0, 2)
    cluster_span = halves * piece_rows
    members = arrived[:halves].reshape(cluster_span, feature_width)
    others = arrived[halves:].reshape(cluster_span, feature_width)
    member_ok = members[:, 0] < 1.5
    other_ok = others[:, 0] < 1.5
    count_own = jnp.sum(member_ok.astype(jnp.float32))
    count_near = jnp.sum(other_ok.astype(jnp.float32))
    sums = lax.dot_general(
        member_ok.astype(jnp.bfloat16)[None, :],
        members,
        (((1,), (0,)), ((), ())),
        preferred_element_type=jnp.float32,
    )
    centroid = normalize(sums)
    typical = TYPICAL_SCALE * jnp.sum(members.astype(jnp.float32) * centroid, axis=1)
    g_own = lax.dot_general(
        members, members, (((1,), (1,)), ((), ())), preferred_element_type=jnp.float32
    )
    g_near = lax.dot_general(
        members, others, (((1,), (1,)), ((), ())), preferred_element_type=jnp.float32
    )
    ids = jnp.arange(cluster_span, dtype=jnp.int32)
    distinct = ids[:, None] != ids[None, :]
    w_own = jnp.where(distinct & member_ok[None, :], jnp.exp(SHARPNESS * g_own), 0.0)
    w_near = jnp.where(other_ok[None, :], jnp.exp(SHARPNESS * g_near), 0.0)
    own_sum = jnp.sum(w_own, axis=1)
    near_sum = jnp.sum(w_near, axis=1)
    score = jnp.log(1.0 + own_sum / count_own + near_sum / count_near)

    def by_source(values):
        return values.reshape(halves, clusters, PIECE).transpose(1, 0, 2).reshape(clusters, MOST)

    payload = jnp.stack([by_source(score), by_source(typical)], axis=1).reshape(clusters, 2 * MOST)
    returned = lax.all_to_all(payload, axes, split_axis=0, concat_axis=0, tiled=True)
    returned = returned.reshape(clusters, 2, MOST)
    home = (row_label * MOST + row_slot)[:, None] == ids[None, :]
    dup_score = jnp.sum(jnp.where(home, returned[:, 0].reshape(-1)[None, :], 0.0), axis=1)
    typical_rows = jnp.sum(jnp.where(home, returned[:, 1].reshape(-1)[None, :], 0.0), axis=1)
    return (dup_score, typical_rows)


def solution(mesh):
    placed = (P(("corpus", "group"), None), P(("corpus", "group"), None), P())
    return jax.shard_map(
        body,
        mesh=mesh,
        in_specs=placed,
        out_specs=(P(("corpus", "group")), P(("corpus", "group"))),
        check_vma=False,
    )
```

```python
import jax
import jax.numpy as jnp
from jax import lax
from jax.sharding import PartitionSpec as P

MOST = 6


SHARPNESS = 16.0
TYPICAL_SCALE = 8.0
EPSILON = 1e-06
EMPTY = 2.0
PIECE = 3


def normalize(values):
    return values * lax.rsqrt(jnp.sum(values * values, axis=-1, keepdims=True) + EPSILON)


def body(embeddings, labels, neighbours):
    axes = ("corpus", "group")
    devices = lax.axis_size("corpus") * lax.axis_size("group")
    row_count, feature_width = embeddings.shape
    clusters = neighbours.shape[0]
    assert clusters == devices
    halves = MOST // PIECE
    pieces = 2 * halves
    piece_rows = clusters * PIECE
    unit_embed = normalize(embeddings).astype(jnp.bfloat16)
    row_label = labels[:, 0]
    cluster_ids = jnp.arange(clusters, dtype=jnp.int32)
    previous = jnp.sum(
        jnp.where(neighbours[None, :] == cluster_ids[:, None], cluster_ids[None, :], 0), axis=1
    )
    row_ids = jnp.arange(row_count, dtype=jnp.int32)
    before = (row_label[None, :] == row_label[:, None]) & (row_ids[None, :] < row_ids[:, None])
    row_slot = jnp.sum(before.astype(jnp.int32), axis=1)
    label_hot = row_label[:, None] == cluster_ids[None, :]
    near_label = jnp.sum(jnp.where(label_hot, previous[None, :], 0), axis=1)
    local_count = jnp.sum(label_hot.astype(jnp.int32), axis=0)
    near_count = jnp.sum(
        jnp.where(neighbours[:, None] == cluster_ids[None, :], local_count[None, :], 0), axis=1
    )

    within = row_slot % PIECE
    half = row_slot // PIECE
    member_pos = half * piece_rows + row_label * PIECE + within
    near_pos = (halves + half) * piece_rows + near_label * PIECE + within
    slot_ids = (
        lax.broadcasted_iota(jnp.int32, (piece_rows, pieces), 1) * piece_rows
        + lax.broadcasted_iota(jnp.int32, (piece_rows, pieces), 0)
    )
    chosen = (member_pos[None, None, :] == slot_ids[:, :, None]) | (
        near_pos[None, None, :] == slot_ids[:, :, None]
    )
    shape3 = (clusters, PIECE, pieces)
    piece_at = lax.broadcasted_iota(jnp.int32, shape3, 2)
    k_at = lax.broadcasted_iota(jnp.int32, shape3, 1)
    have = jnp.where(
        piece_at < halves,
        jnp.broadcast_to(local_count[:, None, None], shape3),
        jnp.broadcast_to(near_count[:, None, None], shape3),
    )
    present = (have > (piece_at % halves) * PIECE + k_at).reshape(piece_rows, pieces)
    picked = lax.dot_general(
        chosen.astype(jnp.bfloat16),
        unit_embed,
        (((2,), (0,)), ((), ())),
        preferred_element_type=jnp.float32,
    )
    first = jnp.arange(feature_width, dtype=jnp.int32)[None, None, :] == 0
    send = jnp.where(first & ~present[:, :, None], EMPTY, picked).astype(jnp.bfloat16)
    arrived = lax.all_to_all(send, axes, split_axis=0, concat_axis=0, tiled=True)
    arrived = arrived.transpose(1, 0, 2)
    cluster_span = halves * piece_rows
    members = arrived[:halves].reshape(cluster_span, feature_width)
    others = arrived[halves:].reshape(cluster_span, feature_width)
    member_ok = members[:, 0] < 1.5
    other_ok = others[:, 0] < 1.5
    count_own = jnp.sum(member_ok.astype(jnp.float32))
    count_near = jnp.sum(other_ok.astype(jnp.float32))
    sums = lax.dot_general(
        member_ok.astype(jnp.bfloat16)[None, :],
        members,
        (((1,), (0,)), ((), ())),
        preferred_element_type=jnp.float32,
    )
    centroid = normalize(sums)
    typical = TYPICAL_SCALE * jnp.sum(members.astype(jnp.float32) * centroid, axis=1)
    g_own = lax.dot_general(
        members, members, (((1,), (1,)), ((), ())), preferred_element_type=jnp.float32
    )
    g_near = lax.dot_general(
        members, others, (((1,), (1,)), ((), ())), preferred_element_type=jnp.float32
    )
    ids = jnp.arange(cluster_span, dtype=jnp.int32)
    distinct = ids[:, None] != ids[None, :]
    w_own = jnp.where(distinct & member_ok[None, :], jnp.exp(SHARPNESS * g_own), 0.0)
    w_near = jnp.where(other_ok[None, :], jnp.exp(SHARPNESS * g_near), 0.0)
    own_sum = jnp.sum(w_own, axis=1)
    near_sum = jnp.sum(w_near, axis=1)
    score = jnp.log(1.0 + own_sum / count_own + near_sum / count_near)

    def by_source(values):
        return values.reshape(halves, clusters, PIECE).transpose(1, 0, 2).reshape(clusters, MOST)

    payload = jnp.stack([by_source(score), by_source(typical)], axis=1).reshape(clusters, 2 * MOST)
    returned = lax.all_to_all(payload, axes, split_axis=0, concat_axis=0, tiled=True)
    returned = returned.reshape(clusters, 2, MOST)
    home = (row_label * MOST + row_slot)[:, None] == ids[None, :]
    dup_score = jnp.sum(jnp.where(home, returned[:, 0].reshape(-1)[None, :], 0.0), axis=1)
    typical_rows = jnp.sum(jnp.where(home, returned[:, 1].reshape(-1)[None, :], 0.0), axis=1)
    return (dup_score, typical_rows)


def solution(mesh):
    placed = (P(("corpus", "group"), None), P(("corpus", "group"), None), P())
    return jax.shard_map(
        body,
        mesh=mesh,
        in_specs=placed,
        out_specs=(P(("corpus", "group")), P(("corpus", "group"))),
        check_vma=False,
    )
```

```python
import jax
import jax.numpy as jnp
from jax import lax
from jax.sharding import PartitionSpec as P

MOST = 6


SHARPNESS = 16.0
TYPICAL_SCALE = 8.0
EPSILON = 1e-06
EMPTY = 2.0
PIECE = 3


def normalize(values):
    return values * lax.rsqrt(jnp.sum(values * values, axis=-1, keepdims=True) + EPSILON)


def body(embeddings, labels, neighbours):
    axes = ("corpus", "group")
    devices = lax.axis_size("corpus") * lax.axis_size("group")
    row_count, feature_width = embeddings.shape
    clusters = neighbours.shape[0]
    assert clusters == devices
    halves = MOST // PIECE
    pieces = 2 * halves
    piece_rows = clusters * PIECE
    unit_embed = normalize(embeddings).astype(jnp.bfloat16)
    row_label = labels[:, 0]
    cluster_ids = jnp.arange(clusters, dtype=jnp.int32)
    previous = jnp.sum(
        jnp.where(neighbours[None, :] == cluster_ids[:, None], cluster_ids[None, :], 0), axis=1
    )
    row_ids = jnp.arange(row_count, dtype=jnp.int32)
    before = (row_label[None, :] == row_label[:, None]) & (row_ids[None, :] < row_ids[:, None])
    row_slot = jnp.sum(before.astype(jnp.int32), axis=1)
    label_hot = row_label[:, None] == cluster_ids[None, :]
    near_label = jnp.sum(jnp.where(label_hot, previous[None, :], 0), axis=1)
    local_count = jnp.sum(label_hot.astype(jnp.int32), axis=0)
    near_count = jnp.sum(
        jnp.where(neighbours[:, None] == cluster_ids[None, :], local_count[None, :], 0), axis=1
    )

    within = row_slot % PIECE
    half = row_slot // PIECE
    member_pos = half * piece_rows + row_label * PIECE + within
    near_pos = (halves + half) * piece_rows + near_label * PIECE + within
    slot_ids = (
        lax.broadcasted_iota(jnp.int32, (piece_rows, pieces), 1) * piece_rows
        + lax.broadcasted_iota(jnp.int32, (piece_rows, pieces), 0)
    )
    chosen = (member_pos[None, None, :] == slot_ids[:, :, None]) | (
        near_pos[None, None, :] == slot_ids[:, :, None]
    )
    shape3 = (clusters, PIECE, pieces)
    piece_at = lax.broadcasted_iota(jnp.int32, shape3, 2)
    k_at = lax.broadcasted_iota(jnp.int32, shape3, 1)
    have = jnp.where(
        piece_at < halves,
        jnp.broadcast_to(local_count[:, None, None], shape3),
        jnp.broadcast_to(near_count[:, None, None], shape3),
    )
    present = (have > (piece_at % halves) * PIECE + k_at).reshape(piece_rows, pieces)
    picked = lax.dot_general(
        chosen.astype(jnp.bfloat16),
        unit_embed,
        (((2,), (0,)), ((), ())),
        preferred_element_type=jnp.float32,
    )
    first = jnp.arange(feature_width, dtype=jnp.int32)[None, None, :] == 0
    send = jnp.where(first & ~present[:, :, None], EMPTY, picked).astype(jnp.bfloat16)
    arrived = lax.all_to_all(send, axes, split_axis=0, concat_axis=0, tiled=True)
    arrived = arrived.transpose(1, 0, 2)
    cluster_span = halves * piece_rows
    members = arrived[:halves].reshape(cluster_span, feature_width)
    others = arrived[halves:].reshape(cluster_span, feature_width)
    member_ok = members[:, 0] < 1.5
    other_ok = others[:, 0] < 1.5
    count_own = jnp.sum(member_ok.astype(jnp.float32))
    count_near = jnp.sum(other_ok.astype(jnp.float32))
    sums = lax.dot_general(
        member_ok.astype(jnp.bfloat16)[None, :],
        members,
        (((1,), (0,)), ((), ())),
        preferred_element_type=jnp.float32,
    )
    centroid = normalize(sums)
    typical = TYPICAL_SCALE * lax.dot_general(
        members.astype(jnp.float32),
        centroid[0],
        (((1,), (0,)), ((), ())),
        precision=lax.Precision.HIGHEST,
        preferred_element_type=jnp.float32,
    )
    g_own = lax.dot_general(
        members, members, (((1,), (1,)), ((), ())), preferred_element_type=jnp.float32
    )
    g_near = lax.dot_general(
        members, others, (((1,), (1,)), ((), ())), preferred_element_type=jnp.float32
    )
    ids = jnp.arange(cluster_span, dtype=jnp.int32)
    distinct = ids[:, None] != ids[None, :]
    w_own = jnp.where(distinct & member_ok[None, :], jnp.exp(SHARPNESS * g_own), 0.0)
    w_near = jnp.where(other_ok[None, :], jnp.exp(SHARPNESS * g_near), 0.0)
    own_sum = jnp.sum(w_own, axis=1)
    near_sum = jnp.sum(w_near, axis=1)
    score = jnp.log(1.0 + own_sum / count_own + near_sum / count_near)

    def by_source(values):
        return values.reshape(halves, clusters, PIECE).transpose(1, 0, 2).reshape(clusters, MOST)

    payload = jnp.stack([by_source(score), by_source(typical)], axis=1).reshape(clusters, 2 * MOST)
    returned = lax.all_to_all(payload, axes, split_axis=0, concat_axis=0, tiled=True)
    returned = returned.reshape(clusters, 2, MOST)
    home = (row_label * MOST + row_slot)[:, None] == ids[None, :]
    dup_score = jnp.sum(jnp.where(home, returned[:, 0].reshape(-1)[None, :], 0.0), axis=1)
    typical_rows = jnp.sum(jnp.where(home, returned[:, 1].reshape(-1)[None, :], 0.0), axis=1)
    return (dup_score, typical_rows)


def solution(mesh):
    placed = (P(("corpus", "group"), None), P(("corpus", "group"), None), P())
    return jax.shard_map(
        body,
        mesh=mesh,
        in_specs=placed,
        out_specs=(P(("corpus", "group")), P(("corpus", "group"))),
        check_vma=False,
    )
```
